512 devices in a mesh: box: 64 (over x, y, z_hi), row: 8 (over z_lo, core).
Axes of the slice: x: 4, y: 8, z: 8 (z_hi: 2, z_lo: 4; z = z_hi * 4 + z_lo), core: 2. Of those that a mesh axis runs over, the one named last changes fastest.
Arguments:
- leaf_maps: float32 [64, 2048, 2048], P('box', 'row'), as said below
- iface_index: int32 [64, 512], replicated, may hold values from 0 to 511, as said below
Outputs:
- merged_maps: bfloat16 [64, 2048, 3072], P('box', 'row')
The draws below stay inside these ranges and needn't reach their ends.
Inputs may be any that keep to these rules, and one draw needn't show every extreme that they name: Each row of iface_index is a permutation of 0 .. 511. Each leaf_maps[c] is exactly symmetric.
All inputs are finite; a program needn't handle non-finite values.
Results may differ from the reference program's by a relative error of at most 0.001.
Values sent between devices are 32-bit elements; how exact they have to be, the bound alone decides.
No kernel may reach another device: no remote copies, remote signals or barrier semaphores. Data moves between devices by JAX's collectives and lax.ppermute only.
A program may use at most 64 MiB of HBM per device.

```python
import jax
import jax.numpy as jnp
from jax import lax

M = 512
BOXES = 64


def interface_order(key):
    keys = jax.random.split(jax.random.fold_in(key, 21), BOXES)
    return jax.vmap(lambda one: jax.random.permutation(one, M))(keys).astype(jnp.int32)


def draw_leaf_maps(key, part):
    key_noise = jax.random.fold_in(key, 11)
    key_diag = jax.random.fold_in(key, 12)
    key_signs = jax.random.fold_in(key, 13)
    entries = jnp.clip(jax.random.normal(key_noise, (BOXES, 4 * M, 4 * M), jnp.float32), -4.0, 4.0)
    diagonal_values = jnp.exp(jax.random.uniform(key_diag, (BOXES, 4 * M), jnp.float32, 0.4054651, 1.7917595))
    common_order = interface_order(key)
    sign_flips = jax.random.randint(key_signs, (BOXES // 2, M), 0, 2).astype(jnp.int32)
    pair_signs = (2 * sign_flips - 1).astype(jnp.float32)
    box_signs = jnp.repeat(pair_signs, 2, axis=0)
    inverse = jnp.argsort(common_order, axis=1, stable=True).astype(jnp.int32)
    placed_signs = jnp.take_along_axis(box_signs, inverse, axis=1)
    diag_signs = jnp.concatenate([jnp.ones((BOXES, 3 * M), jnp.float32), placed_signs], 1)
    diagonal_values = diagonal_values * diag_signs
    positions = jnp.arange(4 * M, dtype=jnp.int32)
    facing = positions >= 3 * M
    both_facing = jnp.logical_and(facing[:, None], facing[None, :])
    same_sign = diag_signs[:, :, None] == diag_signs[:, None, :]
    root_scale = jax.lax.rsqrt(jnp.float32(M))
    within_scale = jnp.float32(0.25) * root_scale
    across_scale = jnp.float32(3.0) * root_scale
    facing_scale = jnp.where(same_sign, within_scale, across_scale)
    scales = jnp.where(both_facing[None, :, :], facing_scale, jnp.float32(0.028284271))
    symmetric = (entries + jnp.swapaxes(entries, 1, 2)) * scales
    identity = (positions[:, None] == positions[None, :]).astype(jnp.float32)
    return symmetric + identity[None, :, :] * diagonal_values[:, :, None]


def draw_iface_index(key, part):
    return interface_order(key)


def setup_inputs(seed: int = 0) -> dict:
    splits = jax.random.split(jax.random.key(seed), 3)
    leaf_maps = draw_leaf_maps(jax.random.fold_in(splits[2], 71), 0)
    iface_index = draw_iface_index(jax.random.fold_in(splits[2], 71), 0)
    return {"leaf_maps": leaf_maps, "iface_index": iface_index}


def merge_pair(operands):
    maps, index = operands
    width = maps.shape[1]
    inner = index.shape[1]
    outer = width - inner
    first = jnp.take(maps[0][:, outer:], index[0], axis=1)
    second = jnp.take(maps[1][:, outer:], index[1], axis=1)
    schur = jnp.take(first[outer:], index[0], axis=0) + jnp.take(second[outer:], index[1], axis=0)
    positions = jnp.arange(width, dtype=jnp.int32)
    unit = (index[0][None, :] == (positions - outer)[:, None]).astype(jnp.float32)
    left_first = jnp.where((positions >= outer)[:, None], unit, first)
    left = jnp.concatenate([left_first, second], 0)
    solved = jnp.linalg.solve(schur, left.T).T
    coupling = jnp.concatenate([first[:outer], second[:outer]], 0)
    update = lax.dot_general(solved, coupling, (((1,), (1,)), ((), ())), precision=lax.Precision.HIGHEST)
    zeros = jnp.zeros((width, outer), jnp.float32)
    keep = jnp.where((positions < outer)[:, None], maps[0][:, :outer], jnp.zeros((), jnp.float32))
    base = jnp.concatenate([jnp.concatenate([keep, zeros], 1), jnp.concatenate([zeros, maps[1][:, :outer]], 1)], 0)
    return (base - update).astype(jnp.bfloat16).reshape(2, width, 2 * outer)

def reference(leaf_maps, iface_index):
    width = leaf_maps.shape[1]
    inner = iface_index.shape[1]
    pairs = leaf_maps.shape[0] // 2
    grouped = leaf_maps.reshape(pairs, 2, width, width)
    indices = iface_index.reshape(pairs, 2, inner)
    merged = lax.map(merge_pair, (grouped, indices))
    return merged.reshape(pairs * 2, width, 6 * inner)
```

```python
import jax
import jax.numpy as jnp
from jax import lax
from jax.sharding import PartitionSpec as P

AXES = ("box", "row")


def ring_pairs(nbox, nrow, shift):
    span = 2 * nrow
    chips = nrow
    pairs = []
    for g in range(nbox * nrow):
        p, q = divmod(g, span)
        z, c = divmod(q, 2)
        pairs.append((g, p * span + 2 * ((z + shift) % chips) + c))
    return pairs


def ring_gather(mine, nbox, nrow):
    chips = nrow
    cw = ring_pairs(nbox, nrow, 1)
    ccw = ring_pairs(nbox, nrow, -1)
    swap = [(g, g ^ 1) for g in range(nbox * nrow)]
    rows = mine.shape[0]
    rel = [None] * chips
    rel[0] = mine
    a = mine
    b = mine
    half = chips // 2
    for k in range(1, (chips - 1) // 2 + 1):
        a = lax.ppermute(a, AXES, cw)
        b = lax.ppermute(b, AXES, ccw)
        rel[k] = a
        rel[chips - k] = b
    if chips % 2 == 0:
        top = lax.ppermute(a[: rows // 2], AXES, cw)
        bot = lax.ppermute(b[rows // 2 :], AXES, ccw)
        rel[half] = jnp.concatenate([top, bot], 0)
    sib = [lax.ppermute(piece, AXES, swap) for piece in rel]
    stacked = jnp.stack(rel + sib)
    q = lax.axis_index("row") + nrow * (lax.axis_index("box") % 2)
    z = q // 2
    c = q % 2
    zs = jnp.arange(chips, dtype=jnp.int32)
    offset = (z - zs) % chips
    idx = jnp.stack([offset + chips * c, offset + chips * (1 - c)], 1).reshape(-1)
    full = jnp.take(stacked, idx, axis=0)
    return full.reshape(chips, 2 * rows, mine.shape[1])


def body(leaf_maps, iface_index):
    local = leaf_maps[0]
    rows_here = local.shape[0]
    width = local.shape[1]
    inner = iface_index.shape[1]
    outer = width - inner
    nbox = lax.axis_size("box")
    nrow = lax.axis_size("row")
    box_id = lax.axis_index("box")
    is_first = box_id % 2 == 0
    first_id = box_id - box_id % 2
    own_index = lax.dynamic_index_in_dim(iface_index, box_id, 0, keepdims=False)
    index_a = lax.dynamic_index_in_dim(iface_index, first_id, 0, keepdims=False)
    index_b = lax.dynamic_index_in_dim(iface_index, first_id + 1, 0, keepdims=False)
    mine = jnp.take(local[:, outer:], own_index, axis=1)
    full = ring_gather(mine, nbox, nrow)
    chips = full.shape[0]
    g_a = full[: chips // 2].reshape(width, inner)
    g_b = full[chips // 2 :].reshape(width, inner)
    schur = jnp.take(g_a[outer:], index_a, axis=0) + jnp.take(g_b[outer:], index_b, axis=0)
    squared = jnp.dot(schur, schur, precision=lax.Precision.HIGHEST)
    factor = jnp.linalg.cholesky(squared)
    first_ext = g_a[:outer]
    second_ext = g_b[:outer]
    global_rows = lax.axis_index("row") * rows_here + jnp.arange(rows_here, dtype=jnp.int32)
    unit = (own_index[None, :] == (global_rows - outer)[:, None]).astype(jnp.float32)
    replaced = jnp.logical_and(is_first, global_rows >= outer)
    left = jnp.where(replaced[:, None], unit, mine)
    local_ext = local[:, :outer]
    zero = jnp.zeros((), jnp.float32)
    left_part = jnp.where(jnp.logical_and(is_first, global_rows < outer)[:, None], local_ext, zero)
    right_part = jnp.where(is_first, zero, local_ext)
    base = jnp.concatenate([left_part, right_part], 1)
    turned = jnp.dot(schur, left.T, precision=lax.Precision.HIGHEST)
    solved = jax.scipy.linalg.cho_solve((factor, True), turned).T
    contract = (((1,), (1,)), ((), ()))
    update_first = lax.dot_general(solved, first_ext, contract, precision=lax.Precision.HIGHEST)
    update_second = lax.dot_general(solved, second_ext, contract, precision=lax.Precision.HIGHEST)
    merged = base - jnp.concatenate([update_first, update_second], 1)
    return merged.astype(jnp.bfloat16)[None]


def solution(mesh):
    in_specs = (P("box", "row", None), P())
    out_specs = P("box", "row", None)
    return jax.shard_map(body, mesh=mesh, in_specs=in_specs, out_specs=out_specs, check_vma=False)
```

```python
import jax
import jax.numpy as jnp
from jax import lax
from jax.experimental import pallas as pl
from jax.experimental.pallas import tpu as pltpu
from jax.sharding import PartitionSpec as P

AXES = ("box", "row")
HI = lax.Precision.HIGHEST


def _gj_kernel(a_ref, o_ref, p_ref):
    n = a_ref.shape[0]
    nb = p_ref.shape[0]
    o_ref[...] = a_ref[...]
    lane_p = lax.broadcasted_iota(jnp.int32, (nb, nb), 1)
    lane_r = lax.broadcasted_iota(jnp.int32, (1, nb), 1)
    sub_c = lax.broadcasted_iota(jnp.int32, (nb, 1), 0)
    for kb in range(n // nb):
        lo = kb * nb
        p_ref[...] = o_ref[lo:lo + nb, lo:lo + nb]

        def step(j, carry):
            block = p_ref[...]
            row = p_ref[pl.ds(j, 1), :]
            piv = jnp.sum(jnp.where(lane_r == j, row, 0.0), axis=1, keepdims=True)
            inv = 1.0 / piv
            rnew = jnp.where(lane_r == j, 1.0, row) * inv
            col = jnp.sum(jnp.where(lane_p == j, block, 0.0), axis=1, keepdims=True)
            col = jnp.where(sub_c == j, 0.0, col)
            p_ref[...] = jnp.where(lane_p == j, 0.0, block) - col * rnew
            p_ref[pl.ds(j, 1), :] = rnew
            return carry

        lax.fori_loop(0, nb, step, 0)
        pinv = p_ref[...]
        lane_n = lax.broadcasted_iota(jnp.int32, (nb, n), 1)
        sub_n = lax.broadcasted_iota(jnp.int32, (nb, n), 0)
        in_cols = jnp.logical_and(lane_n >= lo, lane_n < lo + nb)
        eye = jnp.where(lane_n - lo == sub_n, 1.0, 0.0)
        rows = jnp.where(in_cols, eye, o_ref[lo:lo + nb, :])
        rnew = jnp.dot(pinv, rows, precision=HI, preferred_element_type=jnp.float32)
        sub_k = lax.broadcasted_iota(jnp.int32, (n, nb), 0)
        cols = jnp.where(jnp.logical_and(sub_k >= lo, sub_k < lo + nb), 0.0, o_ref[:, lo:lo + nb])
        lane_a = lax.broadcasted_iota(jnp.int32, (n, n), 1)
        whole = jnp.where(jnp.logical_and(lane_a >= lo, lane_a < lo + nb), 0.0, o_ref[...])
        o_ref[...] = whole - jnp.dot(cols, rnew, precision=HI, preferred_element_type=jnp.float32)
        o_ref[lo:lo + nb, :] = rnew


def spd_inverse(a, nb=128):
    n = a.shape[0]
    return pl.pallas_call(
        _gj_kernel,
        out_shape=jax.ShapeDtypeStruct((n, n), jnp.float32),
        in_specs=[pl.BlockSpec(memory_space=pltpu.VMEM)],
        out_specs=pl.BlockSpec(memory_space=pltpu.VMEM),
        scratch_shapes=[pltpu.VMEM((nb, nb), jnp.float32)],
        cost_estimate=pl.CostEstimate(flops=2 * n * n * n * 6, bytes_accessed=8 * n * n, transcendentals=0),
    )(a)


def ring_pairs(nbox, nrow, shift):
    span = 2 * nrow
    chips = nrow
    pairs = []
    for g in range(nbox * nrow):
        p, q = divmod(g, span)
        z, c = divmod(q, 2)
        pairs.append((g, p * span + 2 * ((z + shift) % chips) + c))
    return pairs


def ring_gather(mine, nbox, nrow):
    chips = nrow
    cw = ring_pairs(nbox, nrow, 1)
    ccw = ring_pairs(nbox, nrow, -1)
    swap = [(g, g ^ 1) for g in range(nbox * nrow)]
    rows = mine.shape[0]
    rel = [None] * chips
    rel[0] = mine
    a = mine
    b = mine
    half = chips // 2
    for k in range(1, (chips - 1) // 2 + 1):
        a = lax.ppermute(a, AXES, cw)
        b = lax.ppermute(b, AXES, ccw)
        rel[k] = a
        rel[chips - k] = b
    if chips % 2 == 0:
        top = lax.ppermute(a[: rows // 2], AXES, cw)
        bot = lax.ppermute(b[rows // 2 :], AXES, ccw)
        rel[half] = jnp.concatenate([top, bot], 0)
    sib = [lax.ppermute(piece, AXES, swap) for piece in rel]
    stacked = jnp.stack(rel + sib)
    q = lax.axis_index("row") + nrow * (lax.axis_index("box") % 2)
    z = q // 2
    c = q % 2
    zs = jnp.arange(chips, dtype=jnp.int32)
    offset = (z - zs) % chips
    idx = jnp.stack([offset + chips * c, offset + chips * (1 - c)], 1).reshape(-1)
    full = jnp.take(stacked, idx, axis=0)
    return full.reshape(chips, 2 * rows, mine.shape[1])


def body(leaf_maps, iface_index):
    local = leaf_maps[0]
    rows_here = local.shape[0]
    width = local.shape[1]
    inner = iface_index.shape[1]
    outer = width - inner
    nbox = lax.axis_size("box")
    nrow = lax.axis_size("row")
    box_id = lax.axis_index("box")
    is_first = box_id % 2 == 0
    first_id = box_id - box_id % 2
    own_index = lax.dynamic_index_in_dim(iface_index, box_id, 0, keepdims=False)
    index_a = lax.dynamic_index_in_dim(iface_index, first_id, 0, keepdims=False)
    index_b = lax.dynamic_index_in_dim(iface_index, first_id + 1, 0, keepdims=False)
    mine = jnp.take(local[:, outer:], own_index, axis=1)
    full = ring_gather(mine, nbox, nrow)
    chips = full.shape[0]
    g_a = full[: chips // 2].reshape(width, inner)
    g_b = full[chips // 2 :].reshape(width, inner)
    schur = jnp.take(g_a[outer:], index_a, axis=0) + jnp.take(g_b[outer:], index_b, axis=0)
    squared = jnp.dot(schur, schur, precision=HI)
    sinv = jnp.dot(spd_inverse(squared), schur, precision=HI)
    first_ext = g_a[:outer]
    second_ext = g_b[:outer]
    global_rows = lax.axis_index("row") * rows_here + jnp.arange(rows_here, dtype=jnp.int32)
    unit = (own_index[None, :] == (global_rows - outer)[:, None]).astype(jnp.float32)
    replaced = jnp.logical_and(is_first, global_rows >= outer)
    left = jnp.where(replaced[:, None], unit, mine)
    local_ext = local[:, :outer]
    zero = jnp.zeros((), jnp.float32)
    left_part = jnp.where(jnp.logical_and(is_first, global_rows < outer)[:, None], local_ext, zero)
    right_part = jnp.where(is_first, zero, local_ext)
    base = jnp.concatenate([left_part, right_part], 1)
    solved = jnp.dot(left, sinv, precision=HI)
    contract = (((1,), (1,)), ((), ()))
    update_first = lax.dot_general(solved, first_ext, contract, precision=lax.Precision.HIGHEST)
    update_second = lax.dot_general(solved, second_ext, contract, precision=lax.Precision.HIGHEST)
    merged = base - jnp.concatenate([update_first, update_second], 1)
    return merged.astype(jnp.bfloat16)[None]


def solution(mesh):
    in_specs = (P("box", "row", None), P())
    out_specs = P("box", "row", None)
    return jax.shard_map(body, mesh=mesh, in_specs=in_specs, out_specs=out_specs, check_vma=False)
```

```python
import jax
import jax.numpy as jnp
from jax import lax
from jax.experimental import pallas as pl
from jax.experimental.pallas import tpu as pltpu
from jax.sharding import PartitionSpec as P

AXES = ("box", "row")
HI = lax.Precision.HIGHEST


def _gj_kernel(a_ref, o_ref, p_ref):
    n = a_ref.shape[0]
    nb = p_ref.shape[0]
    o_ref[...] = a_ref[...]
    lane_p = lax.broadcasted_iota(jnp.int32, (nb, nb), 1)
    lane_r = lax.broadcasted_iota(jnp.int32, (1, nb), 1)
    sub_c = lax.broadcasted_iota(jnp.int32, (nb, 1), 0)
    for kb in range(n // nb):
        lo = kb * nb
        p_ref[...] = o_ref[lo:lo + nb, lo:lo + nb]

        def step(j, carry):
            block = p_ref[...]
            row = p_ref[pl.ds(j, 1), :]
            piv = jnp.sum(jnp.where(lane_r == j, row, 0.0), axis=1, keepdims=True)
            inv = 1.0 / piv
            rnew = jnp.where(lane_r == j, 1.0, row) * inv
            col = jnp.sum(jnp.where(lane_p == j, block, 0.0), axis=1, keepdims=True)
            col = jnp.where(sub_c == j, 0.0, col)
            p_ref[...] = jnp.where(lane_p == j, 0.0, block) - col * rnew
            p_ref[pl.ds(j, 1), :] = rnew
            return carry

        lax.fori_loop(0, nb, step, 0)
        pinv = p_ref[...]
        lane_n = lax.broadcasted_iota(jnp.int32, (nb, n), 1)
        sub_n = lax.broadcasted_iota(jnp.int32, (nb, n), 0)
        in_cols = jnp.logical_and(lane_n >= lo, lane_n < lo + nb)
        eye = jnp.where(lane_n - lo == sub_n, 1.0, 0.0)
        rows = jnp.where(in_cols, eye, o_ref[lo:lo + nb, :])
        rnew = jnp.dot(pinv, rows, precision=HI, preferred_element_type=jnp.float32)
        sub_k = lax.broadcasted_iota(jnp.int32, (n, nb), 0)
        cols = jnp.where(jnp.logical_and(sub_k >= lo, sub_k < lo + nb), 0.0, o_ref[:, lo:lo + nb])
        lane_a = lax.broadcasted_iota(jnp.int32, (n, n), 1)
        whole = jnp.where(jnp.logical_and(lane_a >= lo, lane_a < lo + nb), 0.0, o_ref[...])
        o_ref[...] = whole - jnp.dot(cols, rnew, precision=HI, preferred_element_type=jnp.float32)
        o_ref[lo:lo + nb, :] = rnew


def spd_inverse(a, nb=128):
    n = a.shape[0]
    return pl.pallas_call(
        _gj_kernel,
        out_shape=jax.ShapeDtypeStruct((n, n), jnp.float32),
        in_specs=[pl.BlockSpec(memory_space=pltpu.VMEM)],
        out_specs=pl.BlockSpec(memory_space=pltpu.VMEM),
        scratch_shapes=[pltpu.VMEM((nb, nb), jnp.float32)],
        cost_estimate=pl.CostEstimate(flops=2 * n * n * n * 6, bytes_accessed=8 * n * n, transcendentals=0),
    )(a)


def ring_pairs(nbox, nrow, shift):
    span = 2 * nrow
    chips = nrow
    pairs = []
    for g in range(nbox * nrow):
        p, q = divmod(g, span)
        z, c = divmod(q, 2)
        pairs.append((g, p * span + 2 * ((z + shift) % chips) + c))
    return pairs


def ring_gather(mine, nbox, nrow):
    chips = nrow
    cw = ring_pairs(nbox, nrow, 1)
    ccw = ring_pairs(nbox, nrow, -1)
    swap = [(g, g ^ 1) for g in range(nbox * nrow)]
    rows, cols = mine.shape
    q = lax.axis_index("row") + nrow * (lax.axis_index("box") % 2)
    z = q // 2
    c = q % 2
    rel = [None] * chips
    rel[0] = mine
    a = mine
    b = mine
    done_early = [0]
    for k in range(1, (chips - 1) // 2 + 1):
        a = lax.ppermute(a, AXES, cw)
        b = lax.ppermute(b, AXES, ccw)
        rel[k] = a
        rel[chips - k] = b
        if k <= 2:
            done_early += [k, chips - k]
    if chips % 2 == 0:
        top = lax.ppermute(a[: rows // 2], AXES, cw)
        bot = lax.ppermute(b[rows // 2 :], AXES, ccw)
        rel[chips // 2] = jnp.concatenate([top, bot], 0)
    done_late = [k for k in range(chips) if k not in done_early]
    full = jnp.zeros((2 * chips, rows, cols), mine.dtype)
    for group in (done_early, done_late):
        sib = lax.ppermute(jnp.stack([rel[k] for k in group]), AXES, swap)
        for i, k in enumerate(group):
            slot = 2 * ((z - k) % chips)
            full = lax.dynamic_update_index_in_dim(full, rel[k], slot + c, 0)
            full = lax.dynamic_update_index_in_dim(full, sib[i], slot + 1 - c, 0)
    return full.reshape(chips, 2 * rows, cols)


def body(leaf_maps, iface_index):
    local = leaf_maps[0]
    rows_here = local.shape[0]
    width = local.shape[1]
    inner = iface_index.shape[1]
    outer = width - inner
    nbox = lax.axis_size("box")
    nrow = lax.axis_size("row")
    box_id = lax.axis_index("box")
    is_first = box_id % 2 == 0
    first_id = box_id - box_id % 2
    own_index = lax.dynamic_index_in_dim(iface_index, box_id, 0, keepdims=False)
    index_a = lax.dynamic_index_in_dim(iface_index, first_id, 0, keepdims=False)
    index_b = lax.dynamic_index_in_dim(iface_index, first_id + 1, 0, keepdims=False)
    mine = jnp.take(local[:, outer:], own_index, axis=1)
    full = ring_gather(mine, nbox, nrow)
    chips = full.shape[0]
    g_a = full[: chips // 2].reshape(width, inner)
    g_b = full[chips // 2 :].reshape(width, inner)
    schur = jnp.take(g_a[outer:], index_a, axis=0) + jnp.take(g_b[outer:], index_b, axis=0)
    squared = jnp.dot(schur, schur, precision=HI)
    sinv = jnp.dot(spd_inverse(squared), schur, precision=HI)
    first_ext = g_a[:outer]
    second_ext = g_b[:outer]
    global_rows = lax.axis_index("row") * rows_here + jnp.arange(rows_here, dtype=jnp.int32)
    unit = (own_index[None, :] == (global_rows - outer)[:, None]).astype(jnp.float32)
    replaced = jnp.logical_and(is_first, global_rows >= outer)
    left = jnp.where(replaced[:, None], unit, mine)
    local_ext = local[:, :outer]
    zero = jnp.zeros((), jnp.float32)
    left_part = jnp.where(jnp.logical_and(is_first, global_rows < outer)[:, None], local_ext, zero)
    right_part = jnp.where(is_first, zero, local_ext)
    base = jnp.concatenate([left_part, right_part], 1)
    solved = jnp.dot(left, sinv, precision=HI)
    contract = (((1,), (1,)), ((), ()))
    update_first = lax.dot_general(solved, first_ext, contract, precision=lax.Precision.HIGHEST)
    update_second = lax.dot_general(solved, second_ext, contract, precision=lax.Precision.HIGHEST)
    merged = base - jnp.concatenate([update_first, update_second], 1)
    return merged.astype(jnp.bfloat16)[None]


def solution(mesh):
    in_specs = (P("box", "row", None), P())
    out_specs = P("box", "row", None)
    return jax.shard_map(body, mesh=mesh, in_specs=in_specs, out_specs=out_specs, check_vma=False)
```

```python
import jax
import jax.numpy as jnp
from jax import lax
from jax.experimental import pallas as pl
from jax.experimental.pallas import tpu as pltpu
from jax.sharding import PartitionSpec as P

AXES = ("box", "row")
HI = lax.Precision.HIGHEST


def _panel_inverse(p_ref, s_ref):
    nb = p_ref.shape[0]
    ns = s_ref.shape[0]
    lane_s = lax.broadcasted_iota(jnp.int32, (ns, nb), 1)
    lane_r = lax.broadcasted_iota(jnp.int32, (1, nb), 1)
    sub_c = lax.broadcasted_iota(jnp.int32, (ns, 1), 0)
    sub_p = lax.broadcasted_iota(jnp.int32, (nb, nb), 0)
    lane_p = lax.broadcasted_iota(jnp.int32, (nb, nb), 1)
    for kb in range(nb // ns):
        lo = kb * ns
        s_ref[...] = p_ref[lo:lo + ns, :]

        def step(j, carry):
            pc = lo + j
            slab = s_ref[...]
            row = s_ref[pl.ds(j, 1), :]
            piv = jnp.sum(jnp.where(lane_r == pc, row, 0.0), axis=1, keepdims=True)
            rnew = jnp.where(lane_r == pc, 1.0, row) / piv
            col = jnp.sum(jnp.where(lane_s == pc, slab, 0.0), axis=1, keepdims=True)
            col = jnp.where(sub_c == j, 0.0, col)
            s_ref[...] = jnp.where(lane_s == pc, 0.0, slab) - col * rnew
            s_ref[pl.ds(j, 1), :] = rnew
            return carry

        lax.fori_loop(0, ns, step, 0)
        whole = p_ref[...]
        in_rows = jnp.logical_and(sub_p >= lo, sub_p < lo + ns)
        in_cols = jnp.logical_and(lane_p >= lo, lane_p < lo + ns)
        cols = jnp.where(jnp.logical_and(in_cols, jnp.logical_not(in_rows)), whole, 0.0)
        p_ref[lo:lo + ns, :] = s_ref[...]
        e = jnp.where(in_rows, p_ref[...], 0.0)
        upd = jnp.where(in_cols, 0.0, whole) - jnp.dot(cols, e, precision=HI, preferred_element_type=jnp.float32)
        p_ref[...] = jnp.where(in_rows, e, upd)


def _gj_kernel(a_ref, o_ref, p_ref, s_ref):
    n = a_ref.shape[0]
    nb = p_ref.shape[0]
    o_ref[...] = a_ref[...]
    for kb in range(n // nb):
        lo = kb * nb
        p_ref[...] = o_ref[lo:lo + nb, lo:lo + nb]
        _panel_inverse(p_ref, s_ref)
        pinv = p_ref[...]
        lane_n = lax.broadcasted_iota(jnp.int32, (nb, n), 1)
        sub_n = lax.broadcasted_iota(jnp.int32, (nb, n), 0)
        in_cols = jnp.logical_and(lane_n >= lo, lane_n < lo + nb)
        eye = jnp.where(lane_n - lo == sub_n, 1.0, 0.0)
        rows = jnp.where(in_cols, eye, o_ref[lo:lo + nb, :])
        rnew = jnp.dot(pinv, rows, precision=HI, preferred_element_type=jnp.float32)
        sub_k = lax.broadcasted_iota(jnp.int32, (n, nb), 0)
        cols = jnp.where(jnp.logical_and(sub_k >= lo, sub_k < lo + nb), 0.0, o_ref[:, lo:lo + nb])
        lane_a = lax.broadcasted_iota(jnp.int32, (n, n), 1)
        whole = jnp.where(jnp.logical_and(lane_a >= lo, lane_a < lo + nb), 0.0, o_ref[...])
        o_ref[...] = whole - jnp.dot(cols, rnew, precision=HI, preferred_element_type=jnp.float32)
        o_ref[lo:lo + nb, :] = rnew


def spd_inverse(a, nb=128):
    n = a.shape[0]
    return pl.pallas_call(
        _gj_kernel,
        out_shape=jax.ShapeDtypeStruct((n, n), jnp.float32),
        in_specs=[pl.BlockSpec(memory_space=pltpu.VMEM)],
        out_specs=pl.BlockSpec(memory_space=pltpu.VMEM),
        scratch_shapes=[pltpu.VMEM((nb, nb), jnp.float32), pltpu.VMEM((32, nb), jnp.float32)],
        cost_estimate=pl.CostEstimate(flops=2 * n * n * n * 6, bytes_accessed=8 * n * n, transcendentals=0),
    )(a)


def ring_pairs(nbox, nrow, shift):
    span = 2 * nrow
    chips = nrow
    pairs = []
    for g in range(nbox * nrow):
        p, q = divmod(g, span)
        z, c = divmod(q, 2)
        pairs.append((g, p * span + 2 * ((z + shift) % chips) + c))
    return pairs


def ring_gather(mine, nbox, nrow):
    chips = nrow
    cw = ring_pairs(nbox, nrow, 1)
    ccw = ring_pairs(nbox, nrow, -1)
    swap = [(g, g ^ 1) for g in range(nbox * nrow)]
    rows = mine.shape[0]
    rel = [None] * chips
    rel[0] = mine
    a = mine
    b = mine
    half = chips // 2
    for k in range(1, (chips - 1) // 2 + 1):
        a = lax.ppermute(a, AXES, cw)
        b = lax.ppermute(b, AXES, ccw)
        rel[k] = a
        rel[chips - k] = b
    if chips % 2 == 0:
        top = lax.ppermute(a[: rows // 2], AXES, cw)
        bot = lax.ppermute(b[rows // 2 :], AXES, ccw)
        rel[half] = jnp.concatenate([top, bot], 0)
    sib = [lax.ppermute(piece, AXES, swap) for piece in rel]
    stacked = jnp.stack(rel + sib)
    q = lax.axis_index("row") + nrow * (lax.axis_index("box") % 2)
    z = q // 2
    c = q % 2
    zs = jnp.arange(chips, dtype=jnp.int32)
    offset = (z - zs) % chips
    idx = jnp.stack([offset + chips * c, offset + chips * (1 - c)], 1).reshape(-1)
    full = jnp.take(stacked, idx, axis=0)
    return full.reshape(chips, 2 * rows, mine.shape[1])


def body(leaf_maps, iface_index):
    local = leaf_maps[0]
    rows_here = local.shape[0]
    width = local.shape[1]
    inner = iface_index.shape[1]
    outer = width - inner
    nbox = lax.axis_size("box")
    nrow = lax.axis_size("row")
    box_id = lax.axis_index("box")
    is_first = box_id % 2 == 0
    first_id = box_id - box_id % 2
    own_index = lax.dynamic_index_in_dim(iface_index, box_id, 0, keepdims=False)
    index_a = lax.dynamic_index_in_dim(iface_index, first_id, 0, keepdims=False)
    index_b = lax.dynamic_index_in_dim(iface_index, first_id + 1, 0, keepdims=False)
    mine = jnp.take(local[:, outer:], own_index, axis=1)
    full = ring_gather(mine, nbox, nrow)
    chips = full.shape[0]
    g_a = full[: chips // 2].reshape(width, inner)
    g_b = full[chips // 2 :].reshape(width, inner)
    schur = jnp.take(g_a[outer:], index_a, axis=0) + jnp.take(g_b[outer:], index_b, axis=0)
    squared = jnp.dot(schur, schur, precision=HI)
    sinv = jnp.dot(spd_inverse(squared), schur, precision=HI)
    first_ext = g_a[:outer]
    second_ext = g_b[:outer]
    global_rows = lax.axis_index("row") * rows_here + jnp.arange(rows_here, dtype=jnp.int32)
    unit = (own_index[None, :] == (global_rows - outer)[:, None]).astype(jnp.float32)
    replaced = jnp.logical_and(is_first, global_rows >= outer)
    left = jnp.where(replaced[:, None], unit, mine)
    local_ext = local[:, :outer]
    zero = jnp.zeros((), jnp.float32)
    left_part = jnp.where(jnp.logical_and(is_first, global_rows < outer)[:, None], local_ext, zero)
    right_part = jnp.where(is_first, zero, local_ext)
    base = jnp.concatenate([left_part, right_part], 1)
    solved = jnp.dot(left, sinv, precision=HI)
    contract = (((1,), (1,)), ((), ()))
    update_first = lax.dot_general(solved, first_ext, contract, precision=lax.Precision.HIGHEST)
    update_second = lax.dot_general(solved, second_ext, contract, precision=lax.Precision.HIGHEST)
    merged = base - jnp.concatenate([update_first, update_second], 1)
    return merged.astype(jnp.bfloat16)[None]


def solution(mesh):
    in_specs = (P("box", "row", None), P())
    out_specs = P("box", "row", None)
    return jax.shard_map(body, mesh=mesh, in_specs=in_specs, out_specs=out_specs, check_vma=False)
```

```python
import jax
import jax.numpy as jnp
from jax import lax
from jax.experimental import pallas as pl
from jax.experimental.pallas import tpu as pltpu
from jax.sharding import PartitionSpec as P

AXES = ("box", "row")
HI = lax.Precision.HIGHEST


def _gj_kernel(a_ref, o_ref, p_ref):
    n = a_ref.shape[0]
    nb = p_ref.shape[0]
    o_ref[...] = a_ref[...]
    lane_p = lax.broadcasted_iota(jnp.int32, (nb, nb), 1)
    lane_r = lax.broadcasted_iota(jnp.int32, (1, nb), 1)
    sub_c = lax.broadcasted_iota(jnp.int32, (nb, 1), 0)
    for kb in range(n // nb):
        lo = kb * nb
        p_ref[...] = o_ref[lo:lo + nb, lo:lo + nb]

        def step(i, carry):
            j = 2 * i
            block = p_ref[...]
            pair = p_ref[pl.ds(j, 2), :]
            r0 = pair[0:1, :]
            r1 = pair[1:2, :]
            at0 = lane_r == j
            at1 = lane_r == j + 1
            e00 = jnp.sum(jnp.where(at0, r0, 0.0), axis=1, keepdims=True)
            e01 = jnp.sum(jnp.where(at1, r0, 0.0), axis=1, keepdims=True)
            e10 = jnp.sum(jnp.where(at0, r1, 0.0), axis=1, keepdims=True)
            e11 = jnp.sum(jnp.where(at1, r1, 0.0), axis=1, keepdims=True)
            inv_det = 1.0 / (e00 * e11 - e01 * e10)
            m0 = jnp.where(at0, 1.0, jnp.where(at1, 0.0, r0))
            m1 = jnp.where(at0, 0.0, jnp.where(at1, 1.0, r1))
            n0 = (e11 * m0 - e01 * m1) * inv_det
            n1 = (e00 * m1 - e10 * m0) * inv_det
            in_pair = jnp.logical_or(sub_c == j, sub_c == j + 1)
            c0 = jnp.sum(jnp.where(lane_p == j, block, 0.0), axis=1, keepdims=True)
            c1 = jnp.sum(jnp.where(lane_p == j + 1, block, 0.0), axis=1, keepdims=True)
            c0 = jnp.where(in_pair, 0.0, c0)
            c1 = jnp.where(in_pair, 0.0, c1)
            cut = jnp.logical_or(lane_p == j, lane_p == j + 1)
            p_ref[...] = jnp.where(cut, 0.0, block) - c0 * n0 - c1 * n1
            p_ref[pl.ds(j, 2), :] = jnp.concatenate([n0, n1], 0)
            return carry

        lax.fori_loop(0, nb // 2, step, 0)
        pinv = p_ref[...]
        lane_n = lax.broadcasted_iota(jnp.int32, (nb, n), 1)
        sub_n = lax.broadcasted_iota(jnp.int32, (nb, n), 0)
        in_cols = jnp.logical_and(lane_n >= lo, lane_n < lo + nb)
        eye = jnp.where(lane_n - lo == sub_n, 1.0, 0.0)
        rows = jnp.where(in_cols, eye, o_ref[lo:lo + nb, :])
        rnew = jnp.dot(pinv, rows, precision=HI, preferred_element_type=jnp.float32)
        sub_k = lax.broadcasted_iota(jnp.int32, (n, nb), 0)
        cols = jnp.where(jnp.logical_and(sub_k >= lo, sub_k < lo + nb), 0.0, o_ref[:, lo:lo + nb])
        lane_a = lax.broadcasted_iota(jnp.int32, (n, n), 1)
        whole = jnp.where(jnp.logical_and(lane_a >= lo, lane_a < lo + nb), 0.0, o_ref[...])
        o_ref[...] = whole - jnp.dot(cols, rnew, precision=HI, preferred_element_type=jnp.float32)
        o_ref[lo:lo + nb, :] = rnew


def spd_inverse(a, nb=128):
    n = a.shape[0]
    return pl.pallas_call(
        _gj_kernel,
        out_shape=jax.ShapeDtypeStruct((n, n), jnp.float32),
        in_specs=[pl.BlockSpec(memory_space=pltpu.VMEM)],
        out_specs=pl.BlockSpec(memory_space=pltpu.VMEM),
        scratch_shapes=[pltpu.VMEM((nb, nb), jnp.float32)],
        cost_estimate=pl.CostEstimate(flops=2 * n * n * n * 6, bytes_accessed=8 * n * n, transcendentals=0),
    )(a)


def ring_pairs(nbox, nrow, shift):
    span = 2 * nrow
    chips = nrow
    pairs = []
    for g in range(nbox * nrow):
        p, q = divmod(g, span)
        z, c = divmod(q, 2)
        pairs.append((g, p * span + 2 * ((z + shift) % chips) + c))
    return pairs


def ring_gather(mine, nbox, nrow):
    chips = nrow
    cw = ring_pairs(nbox, nrow, 1)
    ccw = ring_pairs(nbox, nrow, -1)
    swap = [(g, g ^ 1) for g in range(nbox * nrow)]
    rows = mine.shape[0]
    rel = [None] * chips
    rel[0] = mine
    a = mine
    b = mine
    half = chips // 2
    for k in range(1, (chips - 1) // 2 + 1):
        a = lax.ppermute(a, AXES, cw)
        b = lax.ppermute(b, AXES, ccw)
        rel[k] = a
        rel[chips - k] = b
    if chips % 2 == 0:
        top = lax.ppermute(a[: rows // 2], AXES, cw)
        bot = lax.ppermute(b[rows // 2 :], AXES, ccw)
        rel[half] = jnp.concatenate([top, bot], 0)
    sib = [lax.ppermute(piece, AXES, swap) for piece in rel]
    stacked = jnp.stack(rel + sib)
    q = lax.axis_index("row") + nrow * (lax.axis_index("box") % 2)
    z = q // 2
    c = q % 2
    zs = jnp.arange(chips, dtype=jnp.int32)
    offset = (z - zs) % chips
    idx = jnp.stack([offset + chips * c, offset + chips * (1 - c)], 1).reshape(-1)
    full = jnp.take(stacked, idx, axis=0)
    return full.reshape(chips, 2 * rows, mine.shape[1])


def body(leaf_maps, iface_index):
    local = leaf_maps[0]
    rows_here = local.shape[0]
    width = local.shape[1]
    inner = iface_index.shape[1]
    outer = width - inner
    nbox = lax.axis_size("box")
    nrow = lax.axis_size("row")
    box_id = lax.axis_index("box")
    is_first = box_id % 2 == 0
    first_id = box_id - box_id % 2
    own_index = lax.dynamic_index_in_dim(iface_index, box_id, 0, keepdims=False)
    index_a = lax.dynamic_index_in_dim(iface_index, first_id, 0, keepdims=False)
    index_b = lax.dynamic_index_in_dim(iface_index, first_id + 1, 0, keepdims=False)
    mine = jnp.take(local[:, outer:], own_index, axis=1)
    full = ring_gather(mine, nbox, nrow)
    chips = full.shape[0]
    g_a = full[: chips // 2].reshape(width, inner)
    g_b = full[chips // 2 :].reshape(width, inner)
    schur = jnp.take(g_a[outer:], index_a, axis=0) + jnp.take(g_b[outer:], index_b, axis=0)
    squared = jnp.dot(schur, schur, precision=HI)
    sinv = jnp.dot(spd_inverse(squared), schur, precision=HI)
    first_ext = g_a[:outer]
    second_ext = g_b[:outer]
    global_rows = lax.axis_index("row") * rows_here + jnp.arange(rows_here, dtype=jnp.int32)
    unit = (own_index[None, :] == (global_rows - outer)[:, None]).astype(jnp.float32)
    replaced = jnp.logical_and(is_first, global_rows >= outer)
    left = jnp.where(replaced[:, None], unit, mine)
    local_ext = local[:, :outer]
    zero = jnp.zeros((), jnp.float32)
    left_part = jnp.where(jnp.logical_and(is_first, global_rows < outer)[:, None], local_ext, zero)
    right_part = jnp.where(is_first, zero, local_ext)
    base = jnp.concatenate([left_part, right_part], 1)
    solved = jnp.dot(left, sinv, precision=HI)
    contract = (((1,), (1,)), ((), ()))
    update_first = lax.dot_general(solved, first_ext, contract, precision=lax.Precision.HIGHEST)
    update_second = lax.dot_general(solved, second_ext, contract, precision=lax.Precision.HIGHEST)
    merged = base - jnp.concatenate([update_first, update_second], 1)
    return merged.astype(jnp.bfloat16)[None]


def solution(mesh):
    in_specs = (P("box", "row", None), P())
    out_specs = P("box", "row", None)
    return jax.shard_map(body, mesh=mesh, in_specs=in_specs, out_specs=out_specs, check_vma=False)
```

```python
import jax
import jax.numpy as jnp
from jax import lax
from jax.experimental import pallas as pl
from jax.experimental.pallas import tpu as pltpu
from jax.sharding import PartitionSpec as P

AXES = ("box", "row")
HI = lax.Precision.HIGHEST


def _panel_kernel(a_ref, p_ref):
    nb = p_ref.shape[0]
    p_ref[...] = a_ref[...]
    lane_p = lax.broadcasted_iota(jnp.int32, (nb, nb), 1)
    lane_r = lax.broadcasted_iota(jnp.int32, (1, nb), 1)
    sub_c = lax.broadcasted_iota(jnp.int32, (nb, 1), 0)

    def step(i, carry):
        j = 2 * i
        block = p_ref[...]
        pair = p_ref[pl.ds(j, 2), :]
        r0 = pair[0:1, :]
        r1 = pair[1:2, :]
        at0 = lane_r == j
        at1 = lane_r == j + 1
        e00 = jnp.sum(jnp.where(at0, r0, 0.0), axis=1, keepdims=True)
        e01 = jnp.sum(jnp.where(at1, r0, 0.0), axis=1, keepdims=True)
        e10 = jnp.sum(jnp.where(at0, r1, 0.0), axis=1, keepdims=True)
        e11 = jnp.sum(jnp.where(at1, r1, 0.0), axis=1, keepdims=True)
        inv_det = 1.0 / (e00 * e11 - e01 * e10)
        m0 = jnp.where(at0, 1.0, jnp.where(at1, 0.0, r0))
        m1 = jnp.where(at0, 0.0, jnp.where(at1, 1.0, r1))
        n0 = (e11 * m0 - e01 * m1) * inv_det
        n1 = (e00 * m1 - e10 * m0) * inv_det
        in_pair = jnp.logical_or(sub_c == j, sub_c == j + 1)
        c0 = jnp.sum(jnp.where(lane_p == j, block, 0.0), axis=1, keepdims=True)
        c1 = jnp.sum(jnp.where(lane_p == j + 1, block, 0.0), axis=1, keepdims=True)
        c0 = jnp.where(in_pair, 0.0, c0)
        c1 = jnp.where(in_pair, 0.0, c1)
        cut = jnp.logical_or(lane_p == j, lane_p == j + 1)
        p_ref[...] = jnp.where(cut, 0.0, block) - c0 * n0 - c1 * n1
        p_ref[pl.ds(j, 2), :] = jnp.concatenate([n0, n1], 0)
        return carry

    lax.fori_loop(0, nb // 2, step, 0)


def panel_inverse(a):
    nb = a.shape[0]
    return pl.pallas_call(
        _panel_kernel,
        out_shape=jax.ShapeDtypeStruct((nb, nb), jnp.float32),
        in_specs=[pl.BlockSpec(memory_space=pltpu.VMEM)],
        out_specs=pl.BlockSpec(memory_space=pltpu.VMEM),
        cost_estimate=pl.CostEstimate(flops=2 * nb * nb * nb, bytes_accessed=8 * nb * nb, transcendentals=0),
    )(a)


def spd_inverse(a, nb=128):
    n = a.shape[0]
    eye = jnp.eye(nb, dtype=jnp.float32)
    for kb in range(n // nb):
        lo = kb * nb
        pinv = panel_inverse(a[lo:lo + nb, lo:lo + nb])
        rows = a[lo:lo + nb, :].at[:, lo:lo + nb].set(eye)
        rnew = jnp.dot(pinv, rows, precision=HI)
        cols = a[:, lo:lo + nb].at[lo:lo + nb, :].set(0.0)
        a = a.at[:, lo:lo + nb].set(0.0) - jnp.dot(cols, rnew, precision=HI)
        a = a.at[lo:lo + nb, :].set(rnew)
    return a


def ring_pairs(nbox, nrow, shift):
    span = 2 * nrow
    chips = nrow
    pairs = []
    for g in range(nbox * nrow):
        p, q = divmod(g, span)
        z, c = divmod(q, 2)
        pairs.append((g, p * span + 2 * ((z + shift) % chips) + c))
    return pairs


def ring_gather(mine, nbox, nrow):
    chips = nrow
    cw = ring_pairs(nbox, nrow, 1)
    ccw = ring_pairs(nbox, nrow, -1)
    swap = [(g, g ^ 1) for g in range(nbox * nrow)]
    rows = mine.shape[0]
    rel = [None] * chips
    rel[0] = mine
    a = mine
    b = mine
    half = chips // 2
    for k in range(1, (chips - 1) // 2 + 1):
        a = lax.ppermute(a, AXES, cw)
        b = lax.ppermute(b, AXES, ccw)
        rel[k] = a
        rel[chips - k] = b
    if chips % 2 == 0:
        top = lax.ppermute(a[: rows // 2], AXES, cw)
        bot = lax.ppermute(b[rows // 2 :], AXES, ccw)
        rel[half] = jnp.concatenate([top, bot], 0)
    sib = [lax.ppermute(piece, AXES, swap) for piece in rel]
    stacked = jnp.stack(rel + sib)
    q = lax.axis_index("row") + nrow * (lax.axis_index("box") % 2)
    z = q // 2
    c = q % 2
    zs = jnp.arange(chips, dtype=jnp.int32)
    offset = (z - zs) % chips
    idx = jnp.stack([offset + chips * c, offset + chips * (1 - c)], 1).reshape(-1)
    full = jnp.take(stacked, idx, axis=0)
    return full.reshape(chips, 2 * rows, mine.shape[1])


def body(leaf_maps, iface_index):
    local = leaf_maps[0]
    rows_here = local.shape[0]
    width = local.shape[1]
    inner = iface_index.shape[1]
    outer = width - inner
    nbox = lax.axis_size("box")
    nrow = lax.axis_size("row")
    box_id = lax.axis_index("box")
    is_first = box_id % 2 == 0
    first_id = box_id - box_id % 2
    own_index = lax.dynamic_index_in_dim(iface_index, box_id, 0, keepdims=False)
    index_a = lax.dynamic_index_in_dim(iface_index, first_id, 0, keepdims=False)
    index_b = lax.dynamic_index_in_dim(iface_index, first_id + 1, 0, keepdims=False)
    mine = jnp.take(local[:, outer:], own_index, axis=1)
    full = ring_gather(mine, nbox, nrow)
    chips = full.shape[0]
    g_a = full[: chips // 2].reshape(width, inner)
    g_b = full[chips // 2 :].reshape(width, inner)
    schur = jnp.take(g_a[outer:], index_a, axis=0) + jnp.take(g_b[outer:], index_b, axis=0)
    squared = jnp.dot(schur, schur, precision=HI)
    sinv = jnp.dot(spd_inverse(squared), schur, precision=HI)
    first_ext = g_a[:outer]
    second_ext = g_b[:outer]
    global_rows = lax.axis_index("row") * rows_here + jnp.arange(rows_here, dtype=jnp.int32)
    unit = (own_index[None, :] == (global_rows - outer)[:, None]).astype(jnp.float32)
    replaced = jnp.logical_and(is_first, global_rows >= outer)
    left = jnp.where(replaced[:, None], unit, mine)
    local_ext = local[:, :outer]
    zero = jnp.zeros((), jnp.float32)
    left_part = jnp.where(jnp.logical_and(is_first, global_rows < outer)[:, None], local_ext, zero)
    right_part = jnp.where(is_first, zero, local_ext)
    base = jnp.concatenate([left_part, right_part], 1)
    solved = jnp.dot(left, sinv, precision=HI)
    contract = (((1,), (1,)), ((), ()))
    update_first = lax.dot_general(solved, first_ext, contract, precision=lax.Precision.HIGHEST)
    update_second = lax.dot_general(solved, second_ext, contract, precision=lax.Precision.HIGHEST)
    merged = base - jnp.concatenate([update_first, update_second], 1)
    return merged.astype(jnp.bfloat16)[None]


def solution(mesh):
    in_specs = (P("box", "row", None), P())
    out_specs = P("box", "row", None)
    return jax.shard_map(body, mesh=mesh, in_specs=in_specs, out_specs=out_specs, check_vma=False)
```

```python
import jax
import jax.numpy as jnp
from jax import lax
from jax.experimental import pallas as pl
from jax.experimental.pallas import tpu as pltpu
from jax.sharding import PartitionSpec as P

AXES = ("box", "row")
HI = lax.Precision.HIGHEST


def _gj_kernel(a_ref, o_ref, p_ref):
    n = a_ref.shape[0]
    nb = p_ref.shape[0]
    o_ref[...] = a_ref[...]
    lane_p = lax.broadcasted_iota(jnp.int32, (nb, nb), 1)
    lane_r = lax.broadcasted_iota(jnp.int32, (1, nb), 1)
    sub_c = lax.broadcasted_iota(jnp.int32, (nb, 1), 0)
    for kb in range(n // nb):
        lo = kb * nb
        p_ref[...] = o_ref[lo:lo + nb, lo:lo + nb]

        def step(j, carry):
            block = p_ref[...]
            row = p_ref[pl.ds(j, 1), :]
            piv = jnp.sum(jnp.where(lane_r == j, row, 0.0), axis=1, keepdims=True)
            inv = 1.0 / piv
            rnew = jnp.where(lane_r == j, 1.0, row) * inv
            col = jnp.sum(jnp.where(lane_p == j, block, 0.0), axis=1, keepdims=True)
            col = jnp.where(sub_c == j, 0.0, col)
            p_ref[...] = jnp.where(lane_p == j, 0.0, block) - col * rnew
            p_ref[pl.ds(j, 1), :] = rnew
            return carry

        lax.fori_loop(0, nb, step, 0)
        pinv = p_ref[...]
        lane_n = lax.broadcasted_iota(jnp.int32, (nb, n), 1)
        sub_n = lax.broadcasted_iota(jnp.int32, (nb, n), 0)
        in_cols = jnp.logical_and(lane_n >= lo, lane_n < lo + nb)
        eye = jnp.where(lane_n - lo == sub_n, 1.0, 0.0)
        rows = jnp.where(in_cols, eye, o_ref[lo:lo + nb, :])
        rnew = jnp.dot(pinv, rows, precision=HI, preferred_element_type=jnp.float32)
        sub_k = lax.broadcasted_iota(jnp.int32, (n, nb), 0)
        cols = jnp.where(jnp.logical_and(sub_k >= lo, sub_k < lo + nb), 0.0, o_ref[:, lo:lo + nb])
        lane_a = lax.broadcasted_iota(jnp.int32, (n, n), 1)
        whole = jnp.where(jnp.logical_and(lane_a >= lo, lane_a < lo + nb), 0.0, o_ref[...])
        o_ref[...] = whole - jnp.dot(cols, rnew, precision=HI, preferred_element_type=jnp.float32)
        o_ref[lo:lo + nb, :] = rnew


def spd_inverse(a, nb=128):
    n = a.shape[0]
    return pl.pallas_call(
        _gj_kernel,
        out_shape=jax.ShapeDtypeStruct((n, n), jnp.float32),
        in_specs=[pl.BlockSpec(memory_space=pltpu.VMEM)],
        out_specs=pl.BlockSpec(memory_space=pltpu.VMEM),
        scratch_shapes=[pltpu.VMEM((nb, nb), jnp.float32)],
        cost_estimate=pl.CostEstimate(flops=2 * n * n * n * 6, bytes_accessed=8 * n * n, transcendentals=0),
    )(a)


def ring_pairs(nbox, nrow, shift):
    span = 2 * nrow
    chips = nrow
    pairs = []
    for g in range(nbox * nrow):
        p, q = divmod(g, span)
        z, c = divmod(q, 2)
        pairs.append((g, p * span + 2 * ((z + shift) % chips) + c))
    return pairs


def ring_gather(mine, nbox, nrow):
    chips = nrow
    cw = ring_pairs(nbox, nrow, 1)
    ccw = ring_pairs(nbox, nrow, -1)
    swap = [(g, g ^ 1) for g in range(nbox * nrow)]
    rows = mine.shape[0]
    rel = [None] * chips
    rel[0] = mine
    a = mine
    b = mine
    half = chips // 2
    for k in range(1, (chips - 1) // 2 + 1):
        a = lax.ppermute(a, AXES, cw)
        b = lax.ppermute(b, AXES, ccw)
        rel[k] = a
        rel[chips - k] = b
    if chips % 2 == 0:
        top = lax.ppermute(a[: rows // 2], AXES, cw)
        bot = lax.ppermute(b[rows // 2 :], AXES, ccw)
        rel[half] = jnp.concatenate([top, bot], 0)
    sib = [lax.ppermute(piece, AXES, swap) for piece in rel]
    stacked = jnp.stack(rel + sib)
    q = lax.axis_index("row") + nrow * (lax.axis_index("box") % 2)
    z = q // 2
    c = q % 2
    zs = jnp.arange(chips, dtype=jnp.int32)
    offset = (z - zs) % chips
    idx = jnp.stack([offset + chips * c, offset + chips * (1 - c)], 1).reshape(-1)
    full = jnp.take(stacked, idx, axis=0)
    return full.reshape(chips, 2 * rows, mine.shape[1])


def body(leaf_maps, iface_index):
    local = leaf_maps[0]
    rows_here = local.shape[0]
    width = local.shape[1]
    inner = iface_index.shape[1]
    outer = width - inner
    nbox = lax.axis_size("box")
    nrow = lax.axis_size("row")
    box_id = lax.axis_index("box")
    is_first = box_id % 2 == 0
    first_id = box_id - box_id % 2
    own_index = lax.dynamic_index_in_dim(iface_index, box_id, 0, keepdims=False)
    index_a = lax.dynamic_index_in_dim(iface_index, first_id, 0, keepdims=False)
    index_b = lax.dynamic_index_in_dim(iface_index, first_id + 1, 0, keepdims=False)
    mine = jnp.take(local[:, outer:], own_index, axis=1)
    full = ring_gather(mine, nbox, nrow)
    chips = full.shape[0]
    g_a = full[: chips // 2].reshape(width, inner)
    g_b = full[chips // 2 :].reshape(width, inner)
    schur = jnp.take(g_a[outer:], index_a, axis=0) + jnp.take(g_b[outer:], index_b, axis=0)
    squared = jnp.dot(schur, schur, precision=HI)
    sinv = jnp.dot(spd_inverse(squared), schur, precision=HI)
    first_ext = g_a[:outer]
    second_ext = g_b[:outer]
    global_rows = lax.axis_index("row") * rows_here + jnp.arange(rows_here, dtype=jnp.int32)
    unit = (own_index[None, :] == (global_rows - outer)[:, None]).astype(jnp.float32)
    replaced = jnp.logical_and(is_first, global_rows >= outer)
    left = jnp.where(replaced[:, None], unit, mine)
    local_ext = local[:, :outer]
    zero = jnp.zeros((), jnp.float32)
    left_part = jnp.where(jnp.logical_and(is_first, global_rows < outer)[:, None], local_ext, zero)
    right_part = jnp.where(is_first, zero, local_ext)
    base = jnp.concatenate([left_part, right_part], 1)
    solved = jnp.dot(left, sinv, precision=HI)
    contract = (((1,), (1,)), ((), ()))
    update_first = lax.dot_general(solved, first_ext, contract, precision=lax.Precision.HIGH)
    update_second = lax.dot_general(solved, second_ext, contract, precision=lax.Precision.HIGH)
    merged = base - jnp.concatenate([update_first, update_second], 1)
    return merged.astype(jnp.bfloat16)[None]


def solution(mesh):
    in_specs = (P("box", "row", None), P())
    out_specs = P("box", "row", None)
    return jax.shard_map(body, mesh=mesh, in_specs=in_specs, out_specs=out_specs, check_vma=False)
```

```python
import jax
import jax.numpy as jnp
from jax import lax
from jax.experimental import pallas as pl
from jax.experimental.pallas import tpu as pltpu
from jax.sharding import PartitionSpec as P

AXES = ("box", "row")
HI = lax.Precision.HIGHEST


def _gj_kernel(a_ref, o_ref, p_ref):
    n = a_ref.shape[0]
    nb = p_ref.shape[0]
    o_ref[...] = a_ref[...]
    lane_p = lax.broadcasted_iota(jnp.int32, (nb, nb), 1)
    lane_r = lax.broadcasted_iota(jnp.int32, (1, nb), 1)
    sub_c = lax.broadcasted_iota(jnp.int32, (nb, 1), 0)
    for kb in range(n // nb):
        lo = kb * nb
        p_ref[...] = o_ref[lo:lo + nb, lo:lo + nb]

        def step(j, carry):
            block = p_ref[...]
            row = p_ref[pl.ds(j, 1), :]
            piv = jnp.sum(jnp.where(lane_r == j, row, 0.0), axis=1, keepdims=True)
            inv = 1.0 / piv
            rnew = jnp.where(lane_r == j, 1.0, row) * inv
            col = jnp.sum(jnp.where(lane_p == j, block, 0.0), axis=1, keepdims=True)
            col = jnp.where(sub_c == j, 0.0, col)
            p_ref[...] = jnp.where(lane_p == j, 0.0, block) - col * rnew
            p_ref[pl.ds(j, 1), :] = rnew
            return carry

        lax.fori_loop(0, nb, step, 0)
        pinv = p_ref[...]
        lane_n = lax.broadcasted_iota(jnp.int32, (nb, n), 1)
        sub_n = lax.broadcasted_iota(jnp.int32, (nb, n), 0)
        in_cols = jnp.logical_and(lane_n >= lo, lane_n < lo + nb)
        eye = jnp.where(lane_n - lo == sub_n, 1.0, 0.0)
        rows = jnp.where(in_cols, eye, o_ref[lo:lo + nb, :])
        rnew = jnp.dot(pinv, rows, precision=HI, preferred_element_type=jnp.float32)
        sub_k = lax.broadcasted_iota(jnp.int32, (n, nb), 0)
        cols = jnp.where(jnp.logical_and(sub_k >= lo, sub_k < lo + nb), 0.0, o_ref[:, lo:lo + nb])
        lane_a = lax.broadcasted_iota(jnp.int32, (n, n), 1)
        whole = jnp.where(jnp.logical_and(lane_a >= lo, lane_a < lo + nb), 0.0, o_ref[...])
        o_ref[...] = whole - jnp.dot(cols, rnew, precision=HI, preferred_element_type=jnp.float32)
        o_ref[lo:lo + nb, :] = rnew


def spd_inverse(a, nb=128):
    n = a.shape[0]
    return pl.pallas_call(
        _gj_kernel,
        out_shape=jax.ShapeDtypeStruct((n, n), jnp.float32),
        in_specs=[pl.BlockSpec(memory_space=pltpu.VMEM)],
        out_specs=pl.BlockSpec(memory_space=pltpu.VMEM),
        scratch_shapes=[pltpu.VMEM((nb, nb), jnp.float32)],
        cost_estimate=pl.CostEstimate(flops=2 * n * n * n * 6, bytes_accessed=8 * n * n, transcendentals=0),
    )(a)


def ring_pairs(nbox, nrow, shift):
    span = 2 * nrow
    chips = nrow
    pairs = []
    for g in range(nbox * nrow):
        p, q = divmod(g, span)
        z, c = divmod(q, 2)
        pairs.append((g, p * span + 2 * ((z + shift) % chips) + c))
    return pairs


def ring_gather(mine, nbox, nrow):
    chips = nrow
    cw = ring_pairs(nbox, nrow, 1)
    ccw = ring_pairs(nbox, nrow, -1)
    swap = [(g, g ^ 1) for g in range(nbox * nrow)]
    rows = mine.shape[0]
    rel = [None] * chips
    rel[0] = mine
    a = mine
    b = mine
    half = chips // 2
    for k in range(1, (chips - 1) // 2 + 1):
        a = lax.ppermute(a, AXES, cw)
        b = lax.ppermute(b, AXES, ccw)
        rel[k] = a
        rel[chips - k] = b
    if chips % 2 == 0:
        top = lax.ppermute(a[: rows // 2], AXES, cw)
        bot = lax.ppermute(b[rows // 2 :], AXES, ccw)
        rel[half] = jnp.concatenate([top, bot], 0)
    sib = [lax.ppermute(piece, AXES, swap) for piece in rel]
    stacked = jnp.stack(rel + sib)
    q = lax.axis_index("row") + nrow * (lax.axis_index("box") % 2)
    z = q // 2
    c = q % 2
    zs = jnp.arange(chips, dtype=jnp.int32)
    offset = (z - zs) % chips
    idx = jnp.stack([offset + chips * c, offset + chips * (1 - c)], 1).reshape(-1)
    full = jnp.take(stacked, idx, axis=0)
    return full.reshape(chips, 2 * rows, mine.shape[1])


def body(leaf_maps, iface_index):
    local = leaf_maps[0]
    rows_here = local.shape[0]
    width = local.shape[1]
    inner = iface_index.shape[1]
    outer = width - inner
    nbox = lax.axis_size("box")
    nrow = lax.axis_size("row")
    box_id = lax.axis_index("box")
    is_first = box_id % 2 == 0
    first_id = box_id - box_id % 2
    own_index = lax.dynamic_index_in_dim(iface_index, box_id, 0, keepdims=False)
    index_a = lax.dynamic_index_in_dim(iface_index, first_id, 0, keepdims=False)
    index_b = lax.dynamic_index_in_dim(iface_index, first_id + 1, 0, keepdims=False)
    mine = jnp.take(local[:, outer:], own_index, axis=1)
    full = ring_gather(mine, nbox, nrow)
    chips = full.shape[0]
    g_a = full[: chips // 2].reshape(width, inner)
    g_b = full[chips // 2 :].reshape(width, inner)
    schur = jnp.take(g_a[outer:], index_a, axis=0) + jnp.take(g_b[outer:], index_b, axis=0)
    squared = jnp.dot(schur, schur, precision=HI)
    sinv = jnp.dot(spd_inverse(squared), schur, precision=lax.Precision.HIGH)
    first_ext = g_a[:outer]
    second_ext = g_b[:outer]
    global_rows = lax.axis_index("row") * rows_here + jnp.arange(rows_here, dtype=jnp.int32)
    unit = (own_index[None, :] == (global_rows - outer)[:, None]).astype(jnp.float32)
    replaced = jnp.logical_and(is_first, global_rows >= outer)
    left = jnp.where(replaced[:, None], unit, mine)
    local_ext = local[:, :outer]
    zero = jnp.zeros((), jnp.float32)
    left_part = jnp.where(jnp.logical_and(is_first, global_rows < outer)[:, None], local_ext, zero)
    right_part = jnp.where(is_first, zero, local_ext)
    base = jnp.concatenate([left_part, right_part], 1)
    solved = jnp.dot(left, sinv, precision=lax.Precision.HIGH)
    contract = (((1,), (1,)), ((), ()))
    update_first = lax.dot_general(solved, first_ext, contract, precision=lax.Precision.HIGH)
    update_second = lax.dot_general(solved, second_ext, contract, precision=lax.Precision.HIGH)
    merged = base - jnp.concatenate([update_first, update_second], 1)
    return merged.astype(jnp.bfloat16)[None]


def solution(mesh):
    in_specs = (P("box", "row", None), P())
    out_specs = P("box", "row", None)
    return jax.shard_map(body, mesh=mesh, in_specs=in_specs, out_specs=out_specs, check_vma=False)
```
